256 devices in a mesh: seq: 32 (over x, z), mp: 8 (over y, core).
Axes of the slice: x: 4, y: 4, z: 8, core: 2. Of those that a mesh axis runs over, the one named last changes fastest.
Arguments:
- frames: bfloat16 [36864, 1024], P('seq', 'mp'), may hold values from -6 to 6
- keep_flags: int32 [36864], P('seq'), may hold values from 0 to 1, as said below
- pack_rows: int32 [12288], P('seq'), may hold values from 0 to 12287, as said below
- ln_gains: float32 [2, 1024], replicated, may hold values from 0.25 to 1.75
- w_qkv: bfloat16 [1024, 3, 1024], P(None, None, 'mp'), may hold values from -0.1875 to 0.1875, as said below
- w_attn_out: bfloat16 [1024, 1024], P('mp'), may hold values from -0.5 to 0.5
- w_up: bfloat16 [1024, 4096], P(None, 'mp'), may hold values from -0.1875 to 0.1875
- w_down: bfloat16 [4096, 1024], P('mp'), may hold values from -0.09375 to 0.09375
- mask_emb: bfloat16 [1024], replicated, may hold values from -5 to 5
- w_dec_in: bfloat16 [1024, 768], P(None, 'mp'), may hold values from -0.1875 to 0.1875
- w_conv: bfloat16 [4, 7, 768, 48], P(None, None, 'mp'), may hold values from -0.3125 to 0.3125
- w_dec_out: bfloat16 [768, 1024], P('mp'), may hold values from -0.21875 to 0.21875
- targets: bfloat16 [1024, 36864], P('mp', 'seq'), may hold values from -6 to 6
Outputs:
- student_rows: bfloat16 [12288, 1024], P('seq', 'mp')
- pred_error: bfloat16 [1024, 36864], P('mp', 'seq')
The draws below stay inside these ranges and needn't reach their ends.
Inputs may be any that keep to these rules, and one draw needn't show every extreme that they name: `keep_flags`: in each aligned group of four blocks of 1152 frames exactly 1536 frames are kept, and no block keeps more than 768; in some group the first block keeps exactly 768. In all 12288 frames are kept. `pack_rows`: each aligned block of 384 entries is a permutation of the same block of packed rows. `w_qkv`: entries are of the size of a projection with 1024 inputs.
All inputs are finite; a program needn't handle non-finite values.
Results may differ from the reference program's by a relative error of at most 0.019.
Values may be sent and summed in bfloat16 or wider, within the bound.
No kernel may reach another device: no remote copies, remote signals or barrier semaphores. Data moves between devices by JAX's collectives and lax.ppermute only.
A program may use at most 64 MiB of HBM per device.

```python
import math
import jax
import jax.numpy as jnp
from jax import lax

D = 1024
HEADS = 16
HEAD_DIM = 64
FF = 4096
C = 768
GROUPS = 16
CG = 48
KW = 7
BLOCKS = 4
F_DEV = 1152
P_DEV = 384
FRAMES = 36864
KEPT = 12288
N_SEQ = 32
N_MP = 8


def draw_keep_flags(key, part):
    device_count = FRAMES // F_DEV
    group_count = device_count // 4
    key_shift, key_first, key_score = jax.random.split(jax.random.fold_in(key, 101), 3)
    shifts = jax.random.randint(key_shift, (group_count, 4), 0, P_DEV + 1)
    first_group = jax.random.randint(key_first, (), 0, group_count)
    is_first = jnp.arange(group_count)[:, None] == first_group
    column = jnp.arange(4)[None, :]
    shifts = jnp.where(is_first & (column == 0), P_DEV, shifts)
    shifts = jnp.where(is_first & (column == 3), 0, shifts)
    counts = P_DEV + shifts - jnp.roll(shifts, 1, axis=1)
    scores = jax.random.randint(key_score, (device_count, F_DEV), 0, 2 ** 18) * F_DEV + jnp.arange(F_DEV)[None, :]
    order = jnp.argsort(scores, axis=1)
    places = jnp.argsort(order, axis=1)
    flags = (places < counts.reshape(device_count)[:, None]).astype(jnp.int32)
    return flags.reshape(FRAMES)


def draw_pack_rows(key, part):
    device_count = KEPT // P_DEV
    scores = jax.random.randint(jax.random.fold_in(key, 202), (device_count, P_DEV), 0, 2 ** 18) * P_DEV + jnp.arange(P_DEV)[None, :]
    order = jnp.argsort(scores, axis=1).astype(jnp.int32)
    return (order + jnp.arange(device_count, dtype=jnp.int32)[:, None] * P_DEV).reshape(KEPT)


def draw_w_qkv(key, part):
    key_base = jax.random.fold_in(jax.random.fold_in(key, 303), 0)
    key_sharp = jax.random.fold_in(jax.random.fold_in(key, 303), 4)
    limit = 6.0 / math.sqrt(D)
    sharpness = jax.random.uniform(key_sharp, (HEADS,), jnp.float32, 1.8, 2.6)
    head_factor = jnp.repeat(jnp.sqrt(sharpness), HEAD_DIM)
    part_factor = jnp.stack([head_factor, head_factor, jnp.ones((D,), jnp.float32)], axis=0)
    values = jax.random.normal(key_base, (D, 3, D), jnp.float32) / math.sqrt(D) * part_factor[None, :, :]
    return jnp.clip(values, -limit, limit).astype(jnp.bfloat16)


def steps_of(stream_key, extent, cuts, low, top_value):
    def one(dim, shards_of):
        draws = jax.random.uniform(jax.random.fold_in(jax.random.fold_in(stream_key, 6), dim), (shards_of,), jnp.float32, low / len(cuts), top_value / len(cuts))
        return jnp.repeat(jnp.exp(draws), extent[dim] // shards_of).reshape((-1,) + (1,) * (len(extent) - dim - 1))

    level = one(*cuts[0])
    for cut in cuts[1:]:
        level = level * one(*cut)
    return level


def gaussian(rng, shape, scale, most, shards=(), kind=jnp.bfloat16):
    loudness = steps_of(rng, shape, shards, -0.22, 0.18) if shards else 1.0
    drawn = jax.random.normal(rng, shape, jnp.float32) * scale * loudness
    return jnp.minimum(jnp.maximum(drawn, -most), most).astype(kind)


def setup_inputs(seed: int = 0) -> dict:
    streams_of = jax.random.split(jax.random.key(seed), 14)
    frames = gaussian(streams_of[0], (FRAMES, D), 1.0, 6.0, ((0, 32), (1, 8)))
    keep_flags = draw_keep_flags(jax.random.fold_in(streams_of[13], 71), 0)
    pack_rows = draw_pack_rows(jax.random.fold_in(streams_of[13], 71), 0)
    ln_gains = jnp.clip(1.0 + 0.15 * jax.random.normal(streams_of[3], (2, D), jnp.float32), 0.25, 1.75)
    w_qkv = draw_w_qkv(jax.random.fold_in(streams_of[13], 71), 0)
    w_attn_out = gaussian(streams_of[5], (D, D), (D // 8) ** -0.5, 0.5, ((0, 8),))
    w_up = gaussian(streams_of[6], (D, FF), D ** -0.5, 0.1875, ((1, 8),))
    w_down = gaussian(streams_of[7], (FF, D), FF ** -0.5, 0.09375, ((0, 8),))
    mask_emb = gaussian(streams_of[8], (D,), 1.0, 5.0)
    w_dec_in = gaussian(streams_of[9], (D, C), D ** -0.5, 0.1875, ((1, 8),))
    w_conv = gaussian(streams_of[10], (BLOCKS, KW, C, CG), (KW * CG) ** -0.5, 0.3125, ((2, 8),))
    w_dec_out = gaussian(streams_of[11], (C, D), C ** -0.5, 0.21875, ((0, 8),))
    targets = gaussian(streams_of[12], (D, FRAMES), 1.0, 6.0, ((0, 8), (1, 32)))
    return dict(frames=frames, keep_flags=keep_flags, pack_rows=pack_rows, ln_gains=ln_gains, w_qkv=w_qkv, w_attn_out=w_attn_out, w_up=w_up, w_down=w_down, mask_emb=mask_emb, w_dec_in=w_dec_in, w_conv=w_conv, w_dec_out=w_dec_out, targets=targets)


NORM_EPSILON = 1e-05

def layer_norm(values, gain):
    values = values.astype(jnp.float32)
    centre = lax.optimization_barrier(jnp.mean(values, axis=-1, keepdims=True))
    spread = lax.optimization_barrier(jnp.mean(jnp.square(values - centre), axis=-1, keepdims=True))
    return (values - centre) * lax.rsqrt(spread + NORM_EPSILON) * gain

def rounded(values):
    return lax.optimization_barrier(values.astype(jnp.bfloat16)).astype(jnp.float32)

def split_product(left, right):
    part_width = left.shape[1] // N_MP
    total = jnp.zeros((left.shape[0], right.shape[1]), jnp.float32)
    for part_index in range(N_MP):
        lower = part_index * part_width
        piece = jnp.dot(left[:, lower:lower + part_width], right[lower:lower + part_width], preferred_element_type=jnp.float32)
        total = total + rounded(piece)
    return total

def head_attention(query_head, key_head, value_head):
    row_count = query_head.shape[0]
    block_rows = math.gcd(row_count, 512)
    query_blocks = query_head.reshape(row_count // block_rows, block_rows, query_head.shape[1])

    def one_block(query_block):
        scores = jnp.dot(query_block, key_head.T, preferred_element_type=jnp.float32) / math.sqrt(HEAD_DIM)
        highest = lax.optimization_barrier(jnp.max(scores, axis=1, keepdims=True))
        expo = jnp.exp(scores - highest)
        totals = lax.optimization_barrier(jnp.sum(expo, axis=1, keepdims=True))
        return jnp.dot(expo.astype(jnp.bfloat16), value_head, preferred_element_type=jnp.float32) / totals
    return lax.map(one_block, query_blocks).reshape(row_count, query_head.shape[1])

def reference(frames, keep_flags, pack_rows, ln_gains, w_qkv, w_attn_out, w_up, w_down, mask_emb, w_dec_in, w_conv, w_dec_out, targets):
    rank = (jnp.cumsum(keep_flags) - keep_flags).astype(jnp.int32)
    kept_where = jnp.nonzero(keep_flags, size=KEPT)[0].astype(jnp.int32)
    all_ranks = jnp.arange(KEPT, dtype=jnp.int32)
    dealt = (all_ranks % N_SEQ * P_DEV + all_ranks // N_SEQ).astype(jnp.int32)
    dest = pack_rows[dealt].astype(jnp.int32)
    packed = jnp.zeros((KEPT, D), jnp.bfloat16).at[dest].set(frames[kept_where])
    normed = layer_norm(packed, ln_gains[0]).astype(jnp.bfloat16)
    projected = jnp.dot(normed, w_qkv.reshape(D, 3 * D), preferred_element_type=jnp.float32).astype(jnp.bfloat16)
    queries = projected[:, :D].reshape(KEPT, HEADS, HEAD_DIM).transpose(1, 0, 2)
    key_rows = projected[:, D:2 * D].reshape(KEPT, HEADS, HEAD_DIM).transpose(1, 0, 2)
    value_rows = projected[:, 2 * D:].reshape(KEPT, HEADS, HEAD_DIM).transpose(1, 0, 2)
    attended = lax.map(lambda triple: head_attention(triple[0], triple[1], triple[2]), (queries, key_rows, value_rows))
    attended = attended.transpose(1, 0, 2).reshape(KEPT, D).astype(jnp.bfloat16)
    first_out = (packed.astype(jnp.float32) + split_product(attended, w_attn_out)).astype(jnp.bfloat16)
    normed_two = layer_norm(first_out, ln_gains[1]).astype(jnp.bfloat16)
    hidden = jax.nn.gelu(jnp.dot(normed_two, w_up, preferred_element_type=jnp.float32), approximate=False).astype(jnp.bfloat16)
    student_rows = (first_out.astype(jnp.float32) + split_product(hidden, w_down)).astype(jnp.bfloat16)
    by_rank = student_rows[dest]
    safe_rank = jnp.clip(rank, 0, KEPT - 1)
    filled = jnp.where(keep_flags[:, None] == 1, by_rank[safe_rank], mask_emb[None, :])
    activity = jnp.dot(filled, w_dec_in, preferred_element_type=jnp.float32).astype(jnp.bfloat16).T
    for block_id in range(BLOCKS):
        kernel = jnp.transpose(w_conv[block_id].astype(jnp.float32), (1, 2, 0))
        conv = lax.conv_general_dilated(activity.astype(jnp.float32)[None], kernel, (1,), [(KW // 2, KW // 2)], dimension_numbers=('NCH', 'OIH', 'NCH'), feature_group_count=GROUPS, precision=lax.Precision.HIGHEST)[0]
        centre = lax.optimization_barrier(jnp.mean(conv, axis=0))
        square_mean = lax.optimization_barrier(jnp.mean(conv * conv, axis=0))
        normal = (conv - centre) * lax.rsqrt(square_mean - centre * centre + NORM_EPSILON)
        result = jax.nn.gelu(normal, approximate=False)
        if block_id > 0:
            result = result + activity.astype(jnp.float32)
        activity = result.astype(jnp.bfloat16)
    part_height = C // N_MP
    predicted = jnp.zeros((D, FRAMES), jnp.float32)
    for part_index in range(N_MP):
        lower = part_index * part_height
        piece = lax.dot_general(w_dec_out[lower:lower + part_height], activity[lower:lower + part_height], (((0,), (0,)), ((), ())), preferred_element_type=jnp.float32)
        predicted = predicted + rounded(piece)
    masked = (1 - keep_flags).astype(jnp.float32)[None, :]
    pred_error = ((predicted - targets.astype(jnp.float32)) * masked).astype(jnp.bfloat16)
    return (student_rows, pred_error)
```

```python
import math

import jax
import jax.numpy as jnp
from jax import lax
from jax.sharding import PartitionSpec as P

HEAD_DIM = 64
C = 768
CG = 48
KW = 7
BLOCKS = 4


NORM_EPSILON = 1e-05


def with_halo(block, sides, width):
    for axis, dim in sides:
        count = lax.axis_size(axis)
        forward = [(i, i + 1) for i in range(count - 1)]
        backward = [(target, source) for source, target in forward]
        low = lax.ppermute(
            lax.slice_in_dim(block, block.shape[dim] - width, None, axis=dim), axis, forward
        )
        high = lax.ppermute(lax.slice_in_dim(block, 0, width, axis=dim), axis, backward)
        block = jnp.concatenate([low, block, high], axis=dim)
    return block


def gather_all(values, axis):
    count = lax.axis_size(axis)
    spread = jnp.broadcast_to(values[None], (count,) + values.shape)
    return lax.all_to_all(spread, axis, 0, 0, tiled=True)


def sum_scatter(pieces, axis, dim):
    count = lax.axis_size(axis)
    shape = pieces.shape
    split = pieces.reshape(shape[:dim] + (count, shape[dim] // count) + shape[dim + 1 :])
    moved = lax.all_to_all(split, axis, dim, dim, tiled=True)
    return jnp.sum(moved.astype(jnp.float32), axis=dim)


def layer_norm(values, gain):
    values = values.astype(jnp.float32)
    centre = jnp.mean(values, axis=-1, keepdims=True)
    spread = jnp.mean(jnp.square(values - centre), axis=-1, keepdims=True)
    return (values - centre) * lax.rsqrt(spread + NORM_EPSILON) * gain


def rounded(values):
    return lax.optimization_barrier(values.astype(jnp.bfloat16)).astype(jnp.float32)


def local(
    frames,
    keep_flags,
    pack_rows,
    ln_gains,
    w_qkv,
    w_attn_out,
    w_up,
    w_down,
    mask_emb,
    w_dec_in,
    w_conv,
    w_dec_out,
    targets,
):
    frame_count = keep_flags.shape[0]
    slot_rows = pack_rows.shape[0]
    feature_width = frames.shape[1]
    seq_devices = lax.axis_size("seq")
    seq_index = lax.axis_index("seq")
    capacity = (2 * slot_rows + seq_devices - 1) // seq_devices
    kept_count = jnp.sum(keep_flags)
    counts_all = gather_all(kept_count[None], "seq").reshape(seq_devices)
    starts_all = jnp.cumsum(counts_all) - counts_all
    kept_before = starts_all[seq_index]
    local_rank = jnp.cumsum(keep_flags) - keep_flags
    frame_index = jnp.arange(frame_count, dtype=jnp.int32)
    kept_where = (
        jnp.zeros((frame_count,), jnp.int32)
        .at[jnp.where(keep_flags == 1, local_rank, frame_count)]
        .set(frame_index, mode="drop")
    )
    slot_steps = jnp.arange(capacity, dtype=jnp.int32)[None, :] * seq_devices
    owners = jnp.arange(seq_devices, dtype=jnp.int32)
    first_sent = kept_before + (owners - kept_before) % seq_devices
    offset = first_sent[:, None] + slot_steps - kept_before
    inside = offset < kept_count
    source = kept_where[jnp.clip(offset, 0, frame_count - 1)]
    outgoing = jnp.where(inside[..., None], frames[source], jnp.zeros((), jnp.bfloat16))
    incoming = lax.all_to_all(outgoing, "seq", split_axis=0, concat_axis=0, tiled=True)
    first_got = starts_all + (seq_index - starts_all) % seq_devices
    ranks_got = first_got[:, None] + slot_steps
    valid = ranks_got < (starts_all + counts_all)[:, None]
    places = jnp.where(valid, ranks_got // seq_devices, slot_rows).reshape(-1)
    by_rank = (
        jnp.zeros((slot_rows, feature_width), jnp.bfloat16)
        .at[places]
        .set(incoming.reshape(-1, feature_width), mode="drop")
    )
    local_row = pack_rows - seq_index * slot_rows
    inverse = (
        jnp.zeros((slot_rows,), jnp.int32).at[local_row].set(jnp.arange(slot_rows, dtype=jnp.int32))
    )
    packed = by_rank[inverse]
    heads_local = feature_width // HEAD_DIM
    gathered = lax.all_gather(packed, "mp", axis=1, tiled=True)
    normed = layer_norm(gathered, ln_gains[0]).astype(jnp.bfloat16)
    projected = jnp.dot(
        normed, w_qkv.reshape(w_qkv.shape[0], -1), preferred_element_type=jnp.float32
    ).astype(jnp.bfloat16)
    queries = projected[:, :feature_width].reshape(slot_rows, heads_local, HEAD_DIM)
    score_scale = 1.0 / math.sqrt(HEAD_DIM)
    start_state = (
        jnp.full((heads_local, slot_rows), -jnp.inf, jnp.float32),
        jnp.zeros((heads_local, slot_rows), jnp.float32),
        jnp.zeros((slot_rows, heads_local, HEAD_DIM), jnp.float32),
    )
    carry = start_state
    key_value = lax.all_gather(projected[:, feature_width:], "seq", axis=0, tiled=True)
    piece_keys = key_value[:, :feature_width]
    piece_values = key_value[:, feature_width:]
    piece_rows = piece_keys.shape[0]
    block_rows = math.gcd(piece_rows, 512)
    piece_keys = piece_keys.reshape(piece_rows // block_rows, block_rows, heads_local, HEAD_DIM)
    piece_values = piece_values.reshape(piece_rows // block_rows, block_rows, heads_local, HEAD_DIM)

    def advance(state, block_pair):
        running_max, totals, weighted = state
        block_keys, block_values = block_pair
        scores = (
            jnp.einsum("qhd,khd->hqk", queries, block_keys, preferred_element_type=jnp.float32)
            * score_scale
        )
        new_max = jnp.maximum(running_max, jnp.max(scores, axis=2))
        factor = jnp.exp(running_max - new_max)
        expo = jnp.exp(scores - new_max[:, :, None])
        totals = totals * factor + jnp.sum(expo, axis=2)
        weighted = weighted * jnp.transpose(factor)[:, :, None] + jnp.einsum(
            "hqk,khd->qhd",
            expo.astype(jnp.bfloat16),
            block_values,
            preferred_element_type=jnp.float32,
        )
        return ((new_max, totals, weighted), None)

    carry, _ = lax.scan(advance, carry, (piece_keys, piece_values))
    running_max, totals, weighted = carry
    attended = (
        (weighted / jnp.transpose(totals)[:, :, None])
        .reshape(slot_rows, feature_width)
        .astype(jnp.bfloat16)
    )
    attn_terms = rounded(jnp.dot(attended, w_attn_out, preferred_element_type=jnp.float32))
    attn_mixed = sum_scatter(attn_terms.astype(jnp.bfloat16), "mp", 1)
    first_out = (packed.astype(jnp.float32) + attn_mixed).astype(jnp.bfloat16)
    gathered_two = lax.all_gather(first_out, "mp", axis=1, tiled=True)
    normed_two = layer_norm(gathered_two, ln_gains[1]).astype(jnp.bfloat16)
    hidden = jax.nn.gelu(
        jnp.dot(normed_two, w_up, preferred_element_type=jnp.float32), approximate=False
    ).astype(jnp.bfloat16)
    mlp_terms = rounded(jnp.dot(hidden, w_down, preferred_element_type=jnp.float32))
    mlp_mixed = sum_scatter(mlp_terms.astype(jnp.bfloat16), "mp", 1)
    student_rows = (first_out.astype(jnp.float32) + mlp_mixed).astype(jnp.bfloat16)
    filler = lax.dynamic_slice_in_dim(
        mask_emb, lax.axis_index("mp") * feature_width, feature_width, 0
    )
    by_rank_out = student_rows[local_row]
    back_out = by_rank_out[jnp.clip(places, 0, slot_rows - 1)].reshape(
        seq_devices, capacity, feature_width
    )
    back_in = lax.all_to_all(back_out, "seq", 0, 0, tiled=True).reshape(-1, feature_width)
    back_index = ((kept_before + local_rank) % seq_devices) * capacity + local_rank // seq_devices
    returned = back_in[jnp.clip(back_index, 0, seq_devices * capacity - 1)]
    grid_rows = jnp.where(keep_flags[:, None] == 1, returned, filler[None, :])
    grid_whole = lax.all_gather(grid_rows, "mp", axis=1, tiled=True)
    activity = lax.dot_general(
        w_dec_in, grid_whole, (((0,), (1,)), ((), ())), preferred_element_type=jnp.float32
    ).astype(jnp.bfloat16)
    channels_local = activity.shape[0]
    groups_local = channels_local // CG
    for block_id in range(BLOCKS):
        padded = with_halo(activity, (("seq", 1),), KW // 2)
        shifted = jnp.stack(
            [padded[:, tap_index : tap_index + frame_count] for tap_index in range(KW)], axis=0
        )
        shifted = shifted.reshape(KW, groups_local, CG, frame_count)
        kernel = w_conv[block_id].reshape(KW, groups_local, CG, CG)
        conv = jnp.einsum(
            "tgoi,tgif->gof", kernel, shifted, preferred_element_type=jnp.float32
        ).reshape(channels_local, frame_count)
        stats = jnp.stack([jnp.sum(conv, axis=0), jnp.sum(conv * conv, axis=0)], axis=0)
        stats = jnp.sum(gather_all(stats, "mp"), axis=0)
        channel_sums = stats[0]
        square_sums = stats[1]
        centre = channel_sums / C
        square_mean = square_sums / C
        normal = (conv - centre) * lax.rsqrt(square_mean - centre * centre + NORM_EPSILON)
        result = jax.nn.gelu(normal, approximate=False)
        if block_id > 0:
            result = result + activity.astype(jnp.float32)
        activity = result.astype(jnp.bfloat16)
    predicted = sum_scatter(
        rounded(
            lax.dot_general(
                w_dec_out, activity, (((0,), (0,)), ((), ())), preferred_element_type=jnp.float32
            )
        ).astype(jnp.bfloat16),
        "mp",
        0,
    )
    masked = (1 - keep_flags).astype(jnp.float32)[None, :]
    pred_error = ((predicted - targets.astype(jnp.float32)) * masked).astype(jnp.bfloat16)
    return (student_rows, pred_error)


def solution(mesh):
    return jax.shard_map(
        local,
        mesh=mesh,
        in_specs=(
            P("seq", "mp"),
            P("seq"),
            P("seq"),
            P(),
            P(None, None, "mp"),
            P("mp", None),
            P(None, "mp"),
            P("mp", None),
            P(),
            P(None, "mp"),
            P(None, None, "mp", None),
            P("mp", None),
            P("mp", "seq"),
        ),
        out_specs=(P("seq", "mp"), P("mp", "seq")),
        check_vma=False,
    )
```

```python
import math

import jax
import jax.numpy as jnp
from jax import lax
from jax.sharding import PartitionSpec as P

HEAD_DIM = 64
C = 768
CG = 48
KW = 7
BLOCKS = 4


NORM_EPSILON = 1e-05


def with_halo(block, sides, width):
    for axis, dim in sides:
        count = lax.axis_size(axis)
        forward = [(i, i + 1) for i in range(count - 1)]
        backward = [(target, source) for source, target in forward]
        low = lax.ppermute(
            lax.slice_in_dim(block, block.shape[dim] - width, None, axis=dim), axis, forward
        )
        high = lax.ppermute(lax.slice_in_dim(block, 0, width, axis=dim), axis, backward)
        block = jnp.concatenate([low, block, high], axis=dim)
    return block


def gather_all(values, axis):
    count = lax.axis_size(axis)
    spread = jnp.broadcast_to(values[None], (count,) + values.shape)
    return lax.all_to_all(spread, axis, 0, 0, tiled=True)


def sum_scatter(pieces, axis, dim):
    count = lax.axis_size(axis)
    shape = pieces.shape
    split = pieces.reshape(shape[:dim] + (count, shape[dim] // count) + shape[dim + 1 :])
    moved = lax.all_to_all(split, axis, dim, dim, tiled=True)
    return jnp.sum(moved.astype(jnp.float32), axis=dim)


def layer_norm(values, gain):
    values = values.astype(jnp.float32)
    centre = jnp.mean(values, axis=-1, keepdims=True)
    spread = jnp.mean(jnp.square(values - centre), axis=-1, keepdims=True)
    return (values - centre) * lax.rsqrt(spread + NORM_EPSILON) * gain


def rounded(values):
    return lax.optimization_barrier(values.astype(jnp.bfloat16)).astype(jnp.float32)


def local(
    frames,
    keep_flags,
    pack_rows,
    ln_gains,
    w_qkv,
    w_attn_out,
    w_up,
    w_down,
    mask_emb,
    w_dec_in,
    w_conv,
    w_dec_out,
    targets,
):
    frame_count = keep_flags.shape[0]
    slot_rows = pack_rows.shape[0]
    feature_width = frames.shape[1]
    seq_devices = lax.axis_size("seq")
    seq_index = lax.axis_index("seq")
    capacity = (2 * slot_rows + seq_devices - 1) // seq_devices
    kept_count = jnp.sum(keep_flags)
    counts_all = gather_all(kept_count[None], "seq").reshape(seq_devices)
    starts_all = jnp.cumsum(counts_all) - counts_all
    kept_before = starts_all[seq_index]
    local_rank = jnp.cumsum(keep_flags) - keep_flags
    frame_index = jnp.arange(frame_count, dtype=jnp.int32)
    kept_where = (
        jnp.zeros((frame_count,), jnp.int32)
        .at[jnp.where(keep_flags == 1, local_rank, frame_count)]
        .set(frame_index, mode="drop")
    )
    slot_steps = jnp.arange(capacity, dtype=jnp.int32)[None, :] * seq_devices
    owners = jnp.arange(seq_devices, dtype=jnp.int32)
    first_sent = kept_before + (owners - kept_before) % seq_devices
    offset = first_sent[:, None] + slot_steps - kept_before
    inside = offset < kept_count
    source = kept_where[jnp.clip(offset, 0, frame_count - 1)]
    outgoing = jnp.where(inside[..., None], frames[source], jnp.zeros((), jnp.bfloat16))
    incoming = lax.all_to_all(outgoing, "seq", split_axis=0, concat_axis=0, tiled=True)
    first_got = starts_all + (seq_index - starts_all) % seq_devices
    ranks_got = first_got[:, None] + slot_steps
    valid = ranks_got < (starts_all + counts_all)[:, None]
    places = jnp.where(valid, ranks_got // seq_devices, slot_rows).reshape(-1)
    by_rank = (
        jnp.zeros((slot_rows, feature_width), jnp.bfloat16)
        .at[places]
        .set(incoming.reshape(-1, feature_width), mode="drop")
    )
    local_row = pack_rows - seq_index * slot_rows
    inverse = (
        jnp.zeros((slot_rows,), jnp.int32).at[local_row].set(jnp.arange(slot_rows, dtype=jnp.int32))
    )
    packed = by_rank[inverse]
    heads_local = feature_width // HEAD_DIM
    gathered = lax.all_gather(packed, "mp", axis=1, tiled=True)
    normed = layer_norm(gathered, ln_gains[0]).astype(jnp.bfloat16)
    projected = jnp.dot(
        normed, w_qkv.reshape(w_qkv.shape[0], -1), preferred_element_type=jnp.float32
    ).astype(jnp.bfloat16)
    queries = projected[:, :feature_width].reshape(slot_rows, heads_local, HEAD_DIM)
    score_scale = 1.0 / math.sqrt(HEAD_DIM)
    start_state = (
        jnp.full((heads_local, slot_rows), -jnp.inf, jnp.float32),
        jnp.zeros((heads_local, slot_rows), jnp.float32),
        jnp.zeros((slot_rows, heads_local, HEAD_DIM), jnp.float32),
    )
    carry = start_state
    key_value = lax.all_gather(projected[:, feature_width:], "seq", axis=0, tiled=True)
    piece_keys = key_value[:, :feature_width]
    piece_values = key_value[:, feature_width:]
    piece_rows = piece_keys.shape[0]
    block_rows = math.gcd(piece_rows, 512)
    piece_keys = piece_keys.reshape(piece_rows // block_rows, block_rows, heads_local, HEAD_DIM)
    piece_values = piece_values.reshape(piece_rows // block_rows, block_rows, heads_local, HEAD_DIM)

    def advance(state, block_pair):
        running_max, totals, weighted = state
        block_keys, block_values = block_pair
        scores = (
            jnp.einsum("qhd,khd->hqk", queries, block_keys, preferred_element_type=jnp.float32)
            * score_scale
        )
        new_max = jnp.maximum(running_max, jnp.max(scores, axis=2))
        factor = jnp.exp(running_max - new_max)
        expo = jnp.exp(scores - new_max[:, :, None])
        totals = totals * factor + jnp.sum(expo, axis=2)
        weighted = weighted * jnp.transpose(factor)[:, :, None] + jnp.einsum(
            "hqk,khd->qhd",
            expo.astype(jnp.bfloat16),
            block_values,
            preferred_element_type=jnp.float32,
        )
        return ((new_max, totals, weighted), None)

    carry, _ = lax.scan(advance, carry, (piece_keys, piece_values))
    running_max, totals, weighted = carry
    attended = (
        (weighted / jnp.transpose(totals)[:, :, None])
        .reshape(slot_rows, feature_width)
        .astype(jnp.bfloat16)
    )
    attn_terms = rounded(jnp.dot(attended, w_attn_out, preferred_element_type=jnp.float32))
    attn_mixed = sum_scatter(attn_terms.astype(jnp.bfloat16), "mp", 1)
    first_out = (packed.astype(jnp.float32) + attn_mixed).astype(jnp.bfloat16)
    gathered_two = lax.all_gather(first_out, "mp", axis=1, tiled=True)
    normed_two = layer_norm(gathered_two, ln_gains[1]).astype(jnp.bfloat16)
    hidden = jax.nn.gelu(
        jnp.dot(normed_two, w_up, preferred_element_type=jnp.float32), approximate=False
    ).astype(jnp.bfloat16)
    mlp_terms = rounded(jnp.dot(hidden, w_down, preferred_element_type=jnp.float32))
    mlp_mixed = sum_scatter(mlp_terms.astype(jnp.bfloat16), "mp", 1)
    student_rows = (first_out.astype(jnp.float32) + mlp_mixed).astype(jnp.bfloat16)
    filler = lax.dynamic_slice_in_dim(
        mask_emb, lax.axis_index("mp") * feature_width, feature_width, 0
    )
    by_rank_out = student_rows[local_row]
    back_out = by_rank_out[jnp.clip(places, 0, slot_rows - 1)].reshape(
        seq_devices, capacity, feature_width
    )
    back_in = lax.all_to_all(back_out, "seq", 0, 0, tiled=True).reshape(-1, feature_width)
    back_index = ((kept_before + local_rank) % seq_devices) * capacity + local_rank // seq_devices
    returned = back_in[jnp.clip(back_index, 0, seq_devices * capacity - 1)]
    grid_rows = jnp.where(keep_flags[:, None] == 1, returned, filler[None, :])
    mp_devices = lax.axis_size("mp")
    mp_index = lax.axis_index("mp")
    span = frame_count // mp_devices
    halo = (KW // 2) * BLOCKS
    own_frames = lax.all_to_all(
        grid_rows.reshape(mp_devices, span, feature_width), "mp", 0, 2, tiled=True
    ).reshape(span, mp_devices * feature_width)
    dec_in_full = lax.all_gather(w_dec_in, "mp", axis=1, tiled=True)
    conv_full = lax.all_gather(w_conv, "mp", axis=2, tiled=True)
    dec_out_full = lax.all_gather(w_dec_out, "mp", axis=0, tiled=True)
    activity = lax.dot_general(
        dec_in_full, own_frames, (((0,), (1,)), ((), ())), preferred_element_type=jnp.float32
    ).astype(jnp.bfloat16)
    both = ("seq", "mp")
    place = seq_index * mp_devices + mp_index
    places_total = seq_devices * mp_devices
    forward = [(i, i + 1) for i in range(places_total - 1)]
    backward = [(i + 1, i) for i in range(places_total - 1)]
    low = lax.ppermute(activity[:, span - halo :], both, forward)
    high = lax.ppermute(activity[:, :halo], both, backward)
    activity = jnp.concatenate([low, activity, high], axis=1)
    frame_at = place * span - halo + jnp.arange(span + 2 * halo, dtype=jnp.int32)
    in_range = (frame_at >= 0) & (frame_at < places_total * span)
    groups = C // CG
    for block_id in range(BLOCKS):
        width = activity.shape[1] - (KW - 1)
        shifted = jnp.stack(
            [activity[:, tap_index : tap_index + width] for tap_index in range(KW)], axis=0
        ).reshape(KW, groups, CG, width)
        kernel = conv_full[block_id].reshape(KW, groups, CG, CG)
        conv = jnp.einsum(
            "tgoi,tgif->gof", kernel, shifted, preferred_element_type=jnp.float32
        ).reshape(C, width)
        centre = jnp.mean(conv, axis=0)
        square_mean = jnp.mean(conv * conv, axis=0)
        normal = (conv - centre) * lax.rsqrt(square_mean - centre * centre + NORM_EPSILON)
        result = jax.nn.gelu(normal, approximate=False)
        if block_id > 0:
            result = result + activity[:, KW // 2 : KW // 2 + width].astype(jnp.float32)
        lower = (block_id + 1) * (KW // 2)
        result = jnp.where(in_range[lower : lower + width][None, :], result, 0.0)
        activity = result.astype(jnp.bfloat16)
    part_height = C // mp_devices
    pieces = jnp.einsum(
        "jcd,jcf->jdf",
        dec_out_full.reshape(mp_devices, part_height, -1),
        activity.reshape(mp_devices, part_height, span),
        preferred_element_type=jnp.float32,
    )
    predicted = jnp.sum(rounded(pieces), axis=0)
    own_targets = lax.all_to_all(
        targets.reshape(targets.shape[0], mp_devices, span), "mp", 1, 0, tiled=True
    ).reshape(-1, span)
    own_keep = lax.dynamic_slice_in_dim(keep_flags, mp_index * span, span, 0)
    masked = (1 - own_keep).astype(jnp.float32)[None, :]
    own_error = ((predicted - own_targets.astype(jnp.float32)) * masked).astype(jnp.bfloat16)
    pred_error = lax.all_to_all(
        own_error.reshape(mp_devices, -1, span), "mp", 0, 2, tiled=True
    ).reshape(-1, frame_count)
    return (student_rows, pred_error)


def solution(mesh):
    return jax.shard_map(
        local,
        mesh=mesh,
        in_specs=(
            P("seq", "mp"),
            P("seq"),
            P("seq"),
            P(),
            P(None, None, "mp"),
            P("mp", None),
            P(None, "mp"),
            P("mp", None),
            P(),
            P(None, "mp"),
            P(None, None, "mp", None),
            P("mp", None),
            P("mp", "seq"),
        ),
        out_specs=(P("seq", "mp"), P("mp", "seq")),
        check_vma=False,
    )
```

```python
import math

import jax
import jax.numpy as jnp
from jax import lax
from jax.sharding import PartitionSpec as P

HEAD_DIM = 64
C = 768
CG = 48
KW = 7
BLOCKS = 4


NORM_EPSILON = 1e-05


def with_halo(block, sides, width):
    for axis, dim in sides:
        count = lax.axis_size(axis)
        forward = [(i, i + 1) for i in range(count - 1)]
        backward = [(target, source) for source, target in forward]
        low = lax.ppermute(
            lax.slice_in_dim(block, block.shape[dim] - width, None, axis=dim), axis, forward
        )
        high = lax.ppermute(lax.slice_in_dim(block, 0, width, axis=dim), axis, backward)
        block = jnp.concatenate([low, block, high], axis=dim)
    return block


def gather_all(values, axis):
    count = lax.axis_size(axis)
    spread = jnp.broadcast_to(values[None], (count,) + values.shape)
    return lax.all_to_all(spread, axis, 0, 0, tiled=True)


def sum_scatter(pieces, axis, dim):
    count = lax.axis_size(axis)
    shape = pieces.shape
    split = pieces.reshape(shape[:dim] + (count, shape[dim] // count) + shape[dim + 1 :])
    moved = lax.all_to_all(split, axis, dim, dim, tiled=True)
    return jnp.sum(moved.astype(jnp.float32), axis=dim)


def layer_norm(values, gain):
    values = values.astype(jnp.float32)
    centre = jnp.mean(values, axis=-1, keepdims=True)
    spread = jnp.mean(jnp.square(values - centre), axis=-1, keepdims=True)
    return (values - centre) * lax.rsqrt(spread + NORM_EPSILON) * gain


def rounded(values):
    return lax.optimization_barrier(values.astype(jnp.bfloat16)).astype(jnp.float32)


def local(
    frames,
    keep_flags,
    pack_rows,
    ln_gains,
    w_qkv,
    w_attn_out,
    w_up,
    w_down,
    mask_emb,
    w_dec_in,
    w_conv,
    w_dec_out,
    targets,
):
    frame_count = keep_flags.shape[0]
    slot_rows = pack_rows.shape[0]
    feature_width = frames.shape[1]
    seq_devices = lax.axis_size("seq")
    seq_index = lax.axis_index("seq")
    capacity = (2 * slot_rows + seq_devices - 1) // seq_devices
    kept_count = jnp.sum(keep_flags)
    counts_all = gather_all(kept_count[None], "seq").reshape(seq_devices)
    starts_all = jnp.cumsum(counts_all) - counts_all
    kept_before = starts_all[seq_index]
    local_rank = jnp.cumsum(keep_flags) - keep_flags
    frame_index = jnp.arange(frame_count, dtype=jnp.int32)
    kept_where = (
        jnp.zeros((frame_count,), jnp.int32)
        .at[jnp.where(keep_flags == 1, local_rank, frame_count)]
        .set(frame_index, mode="drop")
    )
    slot_steps = jnp.arange(capacity, dtype=jnp.int32)[None, :] * seq_devices
    owners = jnp.arange(seq_devices, dtype=jnp.int32)
    first_sent = kept_before + (owners - kept_before) % seq_devices
    offset = first_sent[:, None] + slot_steps - kept_before
    inside = offset < kept_count
    source = kept_where[jnp.clip(offset, 0, frame_count - 1)]
    outgoing = jnp.where(inside[..., None], frames[source], jnp.zeros((), jnp.bfloat16))
    incoming = lax.all_to_all(outgoing, "seq", split_axis=0, concat_axis=0, tiled=True)
    first_got = starts_all + (seq_index - starts_all) % seq_devices
    ranks_got = first_got[:, None] + slot_steps
    valid = ranks_got < (starts_all + counts_all)[:, None]
    places = jnp.where(valid, ranks_got // seq_devices, slot_rows).reshape(-1)
    by_rank = (
        jnp.zeros((slot_rows, feature_width), jnp.bfloat16)
        .at[places]
        .set(incoming.reshape(-1, feature_width), mode="drop")
    )
    local_row = pack_rows - seq_index * slot_rows
    inverse = (
        jnp.zeros((slot_rows,), jnp.int32).at[local_row].set(jnp.arange(slot_rows, dtype=jnp.int32))
    )
    packed = by_rank[inverse]
    heads_local = feature_width // HEAD_DIM
    gathered = lax.all_gather(packed, "mp", axis=1, tiled=True)
    normed = layer_norm(gathered, ln_gains[0]).astype(jnp.bfloat16)
    projected = jnp.dot(
        normed, w_qkv.reshape(w_qkv.shape[0], -1), preferred_element_type=jnp.float32
    ).astype(jnp.bfloat16)
    queries = projected[:, :feature_width].reshape(slot_rows, heads_local, HEAD_DIM)
    score_scale = 1.0 / math.sqrt(HEAD_DIM)
    start_state = (
        jnp.full((heads_local, slot_rows), -jnp.inf, jnp.float32),
        jnp.zeros((heads_local, slot_rows), jnp.float32),
        jnp.zeros((slot_rows, heads_local, HEAD_DIM), jnp.float32),
    )
    carry = start_state
    key_value = lax.all_gather(projected[:, feature_width:], "seq", axis=0, tiled=True)
    piece_keys = key_value[:, :feature_width]
    piece_values = key_value[:, feature_width:]
    piece_rows = piece_keys.shape[0]
    block_rows = math.gcd(piece_rows, 512)
    piece_keys = piece_keys.reshape(piece_rows // block_rows, block_rows, heads_local, HEAD_DIM)
    piece_values = piece_values.reshape(piece_rows // block_rows, block_rows, heads_local, HEAD_DIM)

    def advance(state, block_pair):
        running_max, totals, weighted = state
        block_keys, block_values = block_pair
        scores = (
            jnp.einsum("qhd,khd->hqk", queries, block_keys, preferred_element_type=jnp.float32)
            * score_scale
        )
        new_max = jnp.maximum(running_max, jnp.max(scores, axis=2))
        factor = jnp.exp(running_max - new_max)
        expo = jnp.exp(scores - new_max[:, :, None])
        totals = totals * factor + jnp.sum(expo, axis=2)
        weighted = weighted * jnp.transpose(factor)[:, :, None] + jnp.einsum(
            "hqk,khd->qhd",
            expo.astype(jnp.bfloat16),
            block_values,
            preferred_element_type=jnp.float32,
        )
        return ((new_max, totals, weighted), None)

    carry, _ = lax.scan(advance, carry, (piece_keys, piece_values))
    running_max, totals, weighted = carry
    attended = (
        (weighted / jnp.transpose(totals)[:, :, None])
        .reshape(slot_rows, feature_width)
        .astype(jnp.bfloat16)
    )
    attn_terms = rounded(jnp.dot(attended, w_attn_out, preferred_element_type=jnp.float32))
    attn_mixed = sum_scatter(attn_terms.astype(jnp.bfloat16), "mp", 1)
    first_out = (packed.astype(jnp.float32) + attn_mixed).astype(jnp.bfloat16)
    gathered_two = lax.all_gather(first_out, "mp", axis=1, tiled=True)
    normed_two = layer_norm(gathered_two, ln_gains[1]).astype(jnp.bfloat16)
    hidden = jax.nn.gelu(
        jnp.dot(normed_two, w_up, preferred_element_type=jnp.float32), approximate=False
    ).astype(jnp.bfloat16)
    mlp_terms = rounded(jnp.dot(hidden, w_down, preferred_element_type=jnp.float32))
    mlp_mixed = sum_scatter(mlp_terms.astype(jnp.bfloat16), "mp", 1)
    student_rows = (first_out.astype(jnp.float32) + mlp_mixed).astype(jnp.bfloat16)
    filler = lax.dynamic_slice_in_dim(
        mask_emb, lax.axis_index("mp") * feature_width, feature_width, 0
    )
    by_rank_out = student_rows[local_row]
    back_out = by_rank_out[jnp.clip(places, 0, slot_rows - 1)].reshape(
        seq_devices, capacity, feature_width
    )
    back_in = lax.all_to_all(back_out, "seq", 0, 0, tiled=True).reshape(-1, feature_width)
    back_index = ((kept_before + local_rank) % seq_devices) * capacity + local_rank // seq_devices
    returned = back_in[jnp.clip(back_index, 0, seq_devices * capacity - 1)]
    grid_rows = jnp.where(keep_flags[:, None] == 1, returned, filler[None, :])
    mp_devices = lax.axis_size("mp")
    mp_index = lax.axis_index("mp")
    span = frame_count // mp_devices
    halo = (KW // 2) * BLOCKS
    own_frames = lax.all_to_all(
        grid_rows.reshape(mp_devices, span, feature_width), "mp", 0, 2, tiled=True
    ).reshape(span, mp_devices * feature_width)
    dec_in_full = lax.all_gather(w_dec_in, "mp", axis=1, tiled=True)
    conv_full = lax.all_gather(jnp.transpose(w_conv, (0, 2, 3, 1)), "mp", axis=1, tiled=True)
    dec_out_full = lax.all_gather(w_dec_out, "mp", axis=0, tiled=True)
    activity = lax.dot_general(
        dec_in_full, own_frames, (((0,), (1,)), ((), ())), preferred_element_type=jnp.float32
    ).astype(jnp.bfloat16)
    both = ("seq", "mp")
    place = seq_index * mp_devices + mp_index
    places_total = seq_devices * mp_devices
    forward = [(i, i + 1) for i in range(places_total - 1)]
    backward = [(i + 1, i) for i in range(places_total - 1)]
    low = lax.ppermute(activity[:, span - halo :], both, forward)
    high = lax.ppermute(activity[:, :halo], both, backward)
    activity = jnp.concatenate([low, activity, high], axis=1)
    frame_at = place * span - halo + jnp.arange(span + 2 * halo, dtype=jnp.int32)
    in_range = (frame_at >= 0) & (frame_at < places_total * span)
    groups = C // CG
    for block_id in range(BLOCKS):
        width = activity.shape[1] - (KW - 1)
        conv = lax.conv_general_dilated(
            activity[None],
            conv_full[block_id],
            (1,),
            "VALID",
            dimension_numbers=("NCH", "OIH", "NCH"),
            feature_group_count=groups,
            preferred_element_type=jnp.float32,
        )[0]
        centre = jnp.mean(conv, axis=0)
        square_mean = jnp.mean(conv * conv, axis=0)
        normal = (conv - centre) * lax.rsqrt(square_mean - centre * centre + NORM_EPSILON)
        result = jax.nn.gelu(normal, approximate=False)
        if block_id > 0:
            result = result + activity[:, KW // 2 : KW // 2 + width].astype(jnp.float32)
        lower = (block_id + 1) * (KW // 2)
        result = jnp.where(in_range[lower : lower + width][None, :], result, 0.0)
        activity = result.astype(jnp.bfloat16)
    part_height = C // mp_devices
    pieces = jnp.einsum(
        "jcd,jcf->jdf",
        dec_out_full.reshape(mp_devices, part_height, -1),
        activity.reshape(mp_devices, part_height, span),
        preferred_element_type=jnp.float32,
    )
    predicted = jnp.sum(rounded(pieces), axis=0)
    own_targets = lax.all_to_all(
        targets.reshape(targets.shape[0], mp_devices, span), "mp", 1, 0, tiled=True
    ).reshape(-1, span)
    own_keep = lax.dynamic_slice_in_dim(keep_flags, mp_index * span, span, 0)
    masked = (1 - own_keep).astype(jnp.float32)[None, :]
    own_error = ((predicted - own_targets.astype(jnp.float32)) * masked).astype(jnp.bfloat16)
    pred_error = lax.all_to_all(
        own_error.reshape(mp_devices, -1, span), "mp", 0, 2, tiled=True
    ).reshape(-1, frame_count)
    return (student_rows, pred_error)


def solution(mesh):
    return jax.shard_map(
        local,
        mesh=mesh,
        in_specs=(
            P("seq", "mp"),
            P("seq"),
            P("seq"),
            P(),
            P(None, None, "mp"),
            P("mp", None),
            P(None, "mp"),
            P("mp", None),
            P(),
            P(None, "mp"),
            P(None, None, "mp", None),
            P("mp", None),
            P("mp", "seq"),
        ),
        out_specs=(P("seq", "mp"), P("mp", "seq")),
        check_vma=False,
    )
```

```python
import math

import jax
import jax.numpy as jnp
from jax import lax
from jax.sharding import PartitionSpec as P

HEAD_DIM = 64
C = 768
CG = 48
KW = 7
BLOCKS = 4


NORM_EPSILON = 1e-05


def with_halo(block, sides, width):
    for axis, dim in sides:
        count = lax.axis_size(axis)
        forward = [(i, i + 1) for i in range(count - 1)]
        backward = [(target, source) for source, target in forward]
        low = lax.ppermute(
            lax.slice_in_dim(block, block.shape[dim] - width, None, axis=dim), axis, forward
        )
        high = lax.ppermute(lax.slice_in_dim(block, 0, width, axis=dim), axis, backward)
        block = jnp.concatenate([low, block, high], axis=dim)
    return block


def gather_all(values, axis):
    count = lax.axis_size(axis)
    spread = jnp.broadcast_to(values[None], (count,) + values.shape)
    return lax.all_to_all(spread, axis, 0, 0, tiled=True)


def sum_scatter(pieces, axis, dim):
    count = lax.axis_size(axis)
    shape = pieces.shape
    split = pieces.reshape(shape[:dim] + (count, shape[dim] // count) + shape[dim + 1 :])
    moved = lax.all_to_all(split, axis, dim, dim, tiled=True)
    return jnp.sum(moved.astype(jnp.float32), axis=dim)


def layer_norm(values, gain):
    values = values.astype(jnp.float32)
    centre = jnp.mean(values, axis=-1, keepdims=True)
    spread = jnp.mean(jnp.square(values - centre), axis=-1, keepdims=True)
    return (values - centre) * lax.rsqrt(spread + NORM_EPSILON) * gain


def rounded(values):
    return lax.optimization_barrier(values.astype(jnp.bfloat16)).astype(jnp.float32)


def local(
    frames,
    keep_flags,
    pack_rows,
    ln_gains,
    w_qkv,
    w_attn_out,
    w_up,
    w_down,
    mask_emb,
    w_dec_in,
    w_conv,
    w_dec_out,
    targets,
):
    frame_count = keep_flags.shape[0]
    slot_rows = pack_rows.shape[0]
    feature_width = frames.shape[1]
    seq_devices = lax.axis_size("seq")
    seq_index = lax.axis_index("seq")
    capacity = (2 * slot_rows + seq_devices - 1) // seq_devices
    kept_count = jnp.sum(keep_flags)
    counts_all = gather_all(kept_count[None], "seq").reshape(seq_devices)
    starts_all = jnp.cumsum(counts_all) - counts_all
    kept_before = starts_all[seq_index]
    local_rank = jnp.cumsum(keep_flags) - keep_flags
    frame_index = jnp.arange(frame_count, dtype=jnp.int32)
    kept_where = (
        jnp.zeros((frame_count,), jnp.int32)
        .at[jnp.where(keep_flags == 1, local_rank, frame_count)]
        .set(frame_index, mode="drop")
    )
    slot_steps = jnp.arange(capacity, dtype=jnp.int32)[None, :] * seq_devices
    owners = jnp.arange(seq_devices, dtype=jnp.int32)
    first_sent = kept_before + (owners - kept_before) % seq_devices
    offset = first_sent[:, None] + slot_steps - kept_before
    inside = offset < kept_count
    source = kept_where[jnp.clip(offset, 0, frame_count - 1)]
    outgoing = jnp.where(inside[..., None], frames[source], jnp.zeros((), jnp.bfloat16))
    incoming = lax.all_to_all(outgoing, "seq", split_axis=0, concat_axis=0, tiled=True)
    first_got = starts_all + (seq_index - starts_all) % seq_devices
    ranks_got = first_got[:, None] + slot_steps
    valid = ranks_got < (starts_all + counts_all)[:, None]
    places = jnp.where(valid, ranks_got // seq_devices, slot_rows).reshape(-1)
    by_rank = (
        jnp.zeros((slot_rows, feature_width), jnp.bfloat16)
        .at[places]
        .set(incoming.reshape(-1, feature_width), mode="drop")
    )
    local_row = pack_rows - seq_index * slot_rows
    inverse = (
        jnp.zeros((slot_rows,), jnp.int32).at[local_row].set(jnp.arange(slot_rows, dtype=jnp.int32))
    )
    packed = by_rank[inverse]
    heads_local = feature_width // HEAD_DIM
    gathered = lax.all_gather(packed, "mp", axis=1, tiled=True)
    normed = layer_norm(gathered, ln_gains[0]).astype(jnp.bfloat16)
    projected = jnp.dot(
        normed, w_qkv.reshape(w_qkv.shape[0], -1), preferred_element_type=jnp.float32
    ).astype(jnp.bfloat16)
    queries = projected[:, :feature_width].reshape(slot_rows, heads_local, HEAD_DIM)
    score_scale = 1.0 / math.sqrt(HEAD_DIM)
    start_state = (
        jnp.full((heads_local, slot_rows), -jnp.inf, jnp.float32),
        jnp.zeros((heads_local, slot_rows), jnp.float32),
        jnp.zeros((slot_rows, heads_local, HEAD_DIM), jnp.float32),
    )
    carry = start_state
    key_value = lax.all_gather(projected[:, feature_width:], "seq", axis=0, tiled=True)
    piece_keys = key_value[:, :feature_width]
    piece_values = key_value[:, feature_width:]
    piece_rows = piece_keys.shape[0]
    block_rows = math.gcd(piece_rows, 1024)
    piece_keys = piece_keys.reshape(piece_rows // block_rows, block_rows, heads_local, HEAD_DIM)
    piece_values = piece_values.reshape(piece_rows // block_rows, block_rows, heads_local, HEAD_DIM)

    def advance(state, block_pair):
        running_max, totals, weighted = state
        block_keys, block_values = block_pair
        scores = (
            jnp.einsum("qhd,khd->hqk", queries, block_keys, preferred_element_type=jnp.float32)
            * score_scale
        )
        new_max = jnp.maximum(running_max, jnp.max(scores, axis=2))
        factor = jnp.exp(running_max - new_max)
        expo = jnp.exp(scores - new_max[:, :, None])
        totals = totals * factor + jnp.sum(expo, axis=2)
        weighted = weighted * jnp.transpose(factor)[:, :, None] + jnp.einsum(
            "hqk,khd->qhd",
            expo.astype(jnp.bfloat16),
            block_values,
            preferred_element_type=jnp.float32,
        )
        return ((new_max, totals, weighted), None)

    carry, _ = lax.scan(advance, carry, (piece_keys, piece_values))
    running_max, totals, weighted = carry
    attended = (
        (weighted / jnp.transpose(totals)[:, :, None])
        .reshape(slot_rows, feature_width)
        .astype(jnp.bfloat16)
    )
    attn_terms = rounded(jnp.dot(attended, w_attn_out, preferred_element_type=jnp.float32))
    attn_mixed = sum_scatter(attn_terms.astype(jnp.bfloat16), "mp", 1)
    first_out = (packed.astype(jnp.float32) + attn_mixed).astype(jnp.bfloat16)
    gathered_two = lax.all_gather(first_out, "mp", axis=1, tiled=True)
    normed_two = layer_norm(gathered_two, ln_gains[1]).astype(jnp.bfloat16)
    hidden = jax.nn.gelu(
        jnp.dot(normed_two, w_up, preferred_element_type=jnp.float32), approximate=False
    ).astype(jnp.bfloat16)
    mlp_terms = rounded(jnp.dot(hidden, w_down, preferred_element_type=jnp.float32))
    mlp_mixed = sum_scatter(mlp_terms.astype(jnp.bfloat16), "mp", 1)
    student_rows = (first_out.astype(jnp.float32) + mlp_mixed).astype(jnp.bfloat16)
    filler = lax.dynamic_slice_in_dim(
        mask_emb, lax.axis_index("mp") * feature_width, feature_width, 0
    )
    by_rank_out = student_rows[local_row]
    back_out = by_rank_out[jnp.clip(places, 0, slot_rows - 1)].reshape(
        seq_devices, capacity, feature_width
    )
    back_in = lax.all_to_all(back_out, "seq", 0, 0, tiled=True).reshape(-1, feature_width)
    back_index = ((kept_before + local_rank) % seq_devices) * capacity + local_rank // seq_devices
    returned = back_in[jnp.clip(back_index, 0, seq_devices * capacity - 1)]
    grid_rows = jnp.where(keep_flags[:, None] == 1, returned, filler[None, :])
    mp_devices = lax.axis_size("mp")
    mp_index = lax.axis_index("mp")
    span = frame_count // mp_devices
    halo = (KW // 2) * BLOCKS
    own_frames = lax.all_to_all(
        grid_rows.reshape(mp_devices, span, feature_width), "mp", 0, 2, tiled=True
    ).reshape(span, mp_devices * feature_width)
    dec_in_full = lax.all_gather(w_dec_in, "mp", axis=1, tiled=True)
    conv_full = lax.all_gather(jnp.transpose(w_conv, (0, 2, 1, 3)), "mp", axis=1, tiled=True)
    dec_out_full = lax.all_gather(w_dec_out, "mp", axis=0, tiled=True)
    activity = lax.dot_general(
        dec_in_full, own_frames, (((0,), (1,)), ((), ())), preferred_element_type=jnp.float32
    ).astype(jnp.bfloat16)
    both = ("seq", "mp")
    place = seq_index * mp_devices + mp_index
    places_total = seq_devices * mp_devices
    forward = [(i, i + 1) for i in range(places_total - 1)]
    backward = [(i + 1, i) for i in range(places_total - 1)]
    low = lax.ppermute(activity[:, span - halo :], both, forward)
    high = lax.ppermute(activity[:, :halo], both, backward)
    activity = jnp.concatenate([low, activity, high], axis=1)
    frame_at = place * span - halo + jnp.arange(span + 2 * halo, dtype=jnp.int32)
    in_range = (frame_at >= 0) & (frame_at < places_total * span)
    groups = C // CG
    for block_id in range(BLOCKS):
        width = activity.shape[1] - (KW - 1)
        shifted = jnp.stack(
            [activity[:, tap_index : tap_index + width] for tap_index in range(KW)], axis=0
        ).reshape(KW, groups, CG, width)
        kernel = conv_full[block_id].reshape(groups, CG, KW, CG)
        conv = jnp.einsum(
            "goti,tgif->gof", kernel, shifted, preferred_element_type=jnp.float32
        ).reshape(C, width)
        centre = jnp.mean(conv, axis=0)
        square_mean = jnp.mean(conv * conv, axis=0)
        normal = (conv - centre) * lax.rsqrt(square_mean - centre * centre + NORM_EPSILON)
        result = jax.nn.gelu(normal, approximate=False)
        if block_id > 0:
            result = result + activity[:, KW // 2 : KW // 2 + width].astype(jnp.float32)
        lower = (block_id + 1) * (KW // 2)
        result = jnp.where(in_range[lower : lower + width][None, :], result, 0.0)
        activity = result.astype(jnp.bfloat16)
    part_height = C // mp_devices
    pieces = jnp.einsum(
        "jcd,jcf->jdf",
        dec_out_full.reshape(mp_devices, part_height, -1),
        activity.reshape(mp_devices, part_height, span),
        preferred_element_type=jnp.float32,
    )
    predicted = jnp.sum(rounded(pieces), axis=0)
    own_targets = lax.all_to_all(
        targets.reshape(targets.shape[0], mp_devices, span), "mp", 1, 0, tiled=True
    ).reshape(-1, span)
    own_keep = lax.dynamic_slice_in_dim(keep_flags, mp_index * span, span, 0)
    masked = (1 - own_keep).astype(jnp.float32)[None, :]
    own_error = ((predicted - own_targets.astype(jnp.float32)) * masked).astype(jnp.bfloat16)
    pred_error = lax.all_to_all(
        own_error.reshape(mp_devices, -1, span), "mp", 0, 2, tiled=True
    ).reshape(-1, frame_count)
    return (student_rows, pred_error)


def solution(mesh):
    return jax.shard_map(
        local,
        mesh=mesh,
        in_specs=(
            P("seq", "mp"),
            P("seq"),
            P("seq"),
            P(),
            P(None, None, "mp"),
            P("mp", None),
            P(None, "mp"),
            P("mp", None),
            P(),
            P(None, "mp"),
            P(None, None, "mp", None),
            P("mp", None),
            P("mp", "seq"),
        ),
        out_specs=(P("seq", "mp"), P("mp", "seq")),
        check_vma=False,
    )
```

```python
import math

import jax
import jax.numpy as jnp
from jax import lax
from jax.sharding import PartitionSpec as P

HEAD_DIM = 64
C = 768
CG = 48
KW = 7
BLOCKS = 4


NORM_EPSILON = 1e-05


def with_halo(block, sides, width):
    for axis, dim in sides:
        count = lax.axis_size(axis)
        forward = [(i, i + 1) for i in range(count - 1)]
        backward = [(target, source) for source, target in forward]
        low = lax.ppermute(
            lax.slice_in_dim(block, block.shape[dim] - width, None, axis=dim), axis, forward
        )
        high = lax.ppermute(lax.slice_in_dim(block, 0, width, axis=dim), axis, backward)
        block = jnp.concatenate([low, block, high], axis=dim)
    return block


def gather_all(values, axis):
    count = lax.axis_size(axis)
    spread = jnp.broadcast_to(values[None], (count,) + values.shape)
    return lax.all_to_all(spread, axis, 0, 0, tiled=True)


def sum_scatter(pieces, axis, dim):
    count = lax.axis_size(axis)
    shape = pieces.shape
    split = pieces.reshape(shape[:dim] + (count, shape[dim] // count) + shape[dim + 1 :])
    moved = lax.all_to_all(split, axis, dim, dim, tiled=True)
    return jnp.sum(moved.astype(jnp.float32), axis=dim)


def layer_norm(values, gain):
    values = values.astype(jnp.float32)
    centre = jnp.mean(values, axis=-1, keepdims=True)
    spread = jnp.mean(jnp.square(values - centre), axis=-1, keepdims=True)
    return (values - centre) * lax.rsqrt(spread + NORM_EPSILON) * gain


def rounded(values):
    return lax.optimization_barrier(values.astype(jnp.bfloat16)).astype(jnp.float32)


def local(
    frames,
    keep_flags,
    pack_rows,
    ln_gains,
    w_qkv,
    w_attn_out,
    w_up,
    w_down,
    mask_emb,
    w_dec_in,
    w_conv,
    w_dec_out,
    targets,
):
    frame_count = keep_flags.shape[0]
    slot_rows = pack_rows.shape[0]
    feature_width = frames.shape[1]
    seq_devices = lax.axis_size("seq")
    seq_index = lax.axis_index("seq")
    capacity = (2 * slot_rows + seq_devices - 1) // seq_devices
    kept_count = jnp.sum(keep_flags)
    counts_all = gather_all(kept_count[None], "seq").reshape(seq_devices)
    starts_all = jnp.cumsum(counts_all) - counts_all
    kept_before = starts_all[seq_index]
    local_rank = jnp.cumsum(keep_flags) - keep_flags
    frame_index = jnp.arange(frame_count, dtype=jnp.int32)
    kept_where = (
        jnp.zeros((frame_count,), jnp.int32)
        .at[jnp.where(keep_flags == 1, local_rank, frame_count)]
        .set(frame_index, mode="drop")
    )
    slot_steps = jnp.arange(capacity, dtype=jnp.int32)[None, :] * seq_devices
    owners = jnp.arange(seq_devices, dtype=jnp.int32)
    first_sent = kept_before + (owners - kept_before) % seq_devices
    offset = first_sent[:, None] + slot_steps - kept_before
    inside = offset < kept_count
    source = kept_where[jnp.clip(offset, 0, frame_count - 1)]
    outgoing = jnp.where(inside[..., None], frames[source], jnp.zeros((), jnp.bfloat16))
    incoming = lax.all_to_all(outgoing, "seq", split_axis=0, concat_axis=0, tiled=True)
    first_got = starts_all + (seq_index - starts_all) % seq_devices
    ranks_got = first_got[:, None] + slot_steps
    valid = ranks_got < (starts_all + counts_all)[:, None]
    places = jnp.where(valid, ranks_got // seq_devices, slot_rows).reshape(-1)
    by_rank = (
        jnp.zeros((slot_rows, feature_width), jnp.bfloat16)
        .at[places]
        .set(incoming.reshape(-1, feature_width), mode="drop")
    )
    local_row = pack_rows - seq_index * slot_rows
    inverse = (
        jnp.zeros((slot_rows,), jnp.int32).at[local_row].set(jnp.arange(slot_rows, dtype=jnp.int32))
    )
    packed = by_rank[inverse]
    heads_local = feature_width // HEAD_DIM
    gathered = lax.all_gather(packed, "mp", axis=1, tiled=True)
    normed = layer_norm(gathered, ln_gains[0]).astype(jnp.bfloat16)
    projected = jnp.dot(
        normed, w_qkv.reshape(w_qkv.shape[0], -1), preferred_element_type=jnp.float32
    ).astype(jnp.bfloat16)
    queries = projected[:, :feature_width].reshape(slot_rows, heads_local, HEAD_DIM)
    score_scale = 1.0 / math.sqrt(HEAD_DIM)
    start_state = (
        jnp.full((heads_local, slot_rows), -jnp.inf, jnp.float32),
        jnp.zeros((heads_local, slot_rows), jnp.float32),
        jnp.zeros((slot_rows, heads_local, HEAD_DIM), jnp.float32),
    )
    carry = start_state
    key_value = lax.all_gather(projected[:, feature_width:], "seq", axis=0, tiled=True)
    piece_keys = key_value[:, :feature_width]
    piece_values = key_value[:, feature_width:]
    piece_rows = piece_keys.shape[0]
    block_rows = math.gcd(piece_rows, 512)
    piece_keys = piece_keys.reshape(piece_rows // block_rows, block_rows, heads_local, HEAD_DIM)
    piece_values = piece_values.reshape(piece_rows // block_rows, block_rows, heads_local, HEAD_DIM)

    def advance(state, block_pair):
        running_max, totals, weighted = state
        block_keys, block_values = block_pair
        scores = (
            jnp.einsum("qhd,khd->hqk", queries, block_keys, preferred_element_type=jnp.float32)
            * score_scale
        )
        new_max = jnp.maximum(running_max, jnp.max(scores, axis=2))
        factor = jnp.exp(running_max - new_max)
        expo = jnp.exp(scores - new_max[:, :, None])
        totals = totals * factor + jnp.sum(expo, axis=2)
        weighted = weighted * jnp.transpose(factor)[:, :, None] + jnp.einsum(
            "hqk,khd->qhd",
            expo.astype(jnp.bfloat16),
            block_values,
            preferred_element_type=jnp.float32,
        )
        return ((new_max, totals, weighted), None)

    carry, _ = lax.scan(advance, carry, (piece_keys, piece_values))
    running_max, totals, weighted = carry
    attended = (
        (weighted / jnp.transpose(totals)[:, :, None])
        .reshape(slot_rows, feature_width)
        .astype(jnp.bfloat16)
    )
    attn_terms = rounded(jnp.dot(attended, w_attn_out, preferred_element_type=jnp.float32))
    attn_mixed = sum_scatter(attn_terms.astype(jnp.bfloat16), "mp", 1)
    first_out = (packed.astype(jnp.float32) + attn_mixed).astype(jnp.bfloat16)
    gathered_two = lax.all_gather(first_out, "mp", axis=1, tiled=True)
    normed_two = layer_norm(gathered_two, ln_gains[1]).astype(jnp.bfloat16)
    hidden = jax.nn.gelu(
        jnp.dot(normed_two, w_up, preferred_element_type=jnp.float32), approximate=False
    ).astype(jnp.bfloat16)
    mlp_terms = rounded(jnp.dot(hidden, w_down, preferred_element_type=jnp.float32))
    mlp_mixed = sum_scatter(mlp_terms.astype(jnp.bfloat16), "mp", 1)
    student_rows = (first_out.astype(jnp.float32) + mlp_mixed).astype(jnp.bfloat16)
    filler = lax.dynamic_slice_in_dim(
        mask_emb, lax.axis_index("mp") * feature_width, feature_width, 0
    )
    by_rank_out = student_rows[local_row]
    back_out = by_rank_out[jnp.clip(places, 0, slot_rows - 1)].reshape(
        seq_devices, capacity, feature_width
    )
    back_in = lax.all_to_all(back_out, "seq", 0, 0, tiled=True).reshape(-1, feature_width)
    back_index = ((kept_before + local_rank) % seq_devices) * capacity + local_rank // seq_devices
    returned = back_in[jnp.clip(back_index, 0, seq_devices * capacity - 1)]
    grid_rows = jnp.where(keep_flags[:, None] == 1, returned, filler[None, :])
    mp_devices = lax.axis_size("mp")
    mp_index = lax.axis_index("mp")
    span = frame_count // mp_devices
    halo = (KW // 2) * BLOCKS
    own_frames = lax.all_to_all(
        grid_rows.reshape(mp_devices, span, feature_width), "mp", 0, 2, tiled=True
    ).reshape(span, mp_devices * feature_width)
    dec_in_full = lax.all_gather(w_dec_in, "mp", axis=1, tiled=True)
    conv_full = lax.all_gather(w_conv, "mp", axis=2, tiled=True)
    dec_out_full = lax.all_gather(w_dec_out, "mp", axis=0, tiled=True)
    activity = lax.dot_general(
        dec_in_full, own_frames, (((0,), (1,)), ((), ())), preferred_element_type=jnp.float32
    ).astype(jnp.bfloat16)
    both = ("seq", "mp")
    place = seq_index * mp_devices + mp_index
    places_total = seq_devices * mp_devices
    forward = [(i, i + 1) for i in range(places_total - 1)]
    backward = [(i + 1, i) for i in range(places_total - 1)]
    low = lax.ppermute(activity[:, span - halo :], both, forward)
    high = lax.ppermute(activity[:, :halo], both, backward)
    activity = jnp.concatenate([low, activity, high], axis=1)
    frame_at = place * span - halo + jnp.arange(span + 2 * halo, dtype=jnp.int32)
    in_range = (frame_at >= 0) & (frame_at < places_total * span)
    groups = C // CG
    for block_id in range(BLOCKS):
        width = activity.shape[1] - (KW - 1)
        kernel = conv_full[block_id].reshape(KW, groups, CG, CG)
        conv = jnp.zeros((groups, CG, width), jnp.float32)
        for tap_index in range(KW):
            tap = activity[:, tap_index : tap_index + width].reshape(groups, CG, width)
            conv = conv + jnp.einsum(
                "goi,gif->gof", kernel[tap_index], tap, preferred_element_type=jnp.float32
            )
        conv = conv.reshape(C, width)
        centre = jnp.mean(conv, axis=0)
        square_mean = jnp.mean(conv * conv, axis=0)
        normal = (conv - centre) * lax.rsqrt(square_mean - centre * centre + NORM_EPSILON)
        result = jax.nn.gelu(normal, approximate=False)
        if block_id > 0:
            result = result + activity[:, KW // 2 : KW // 2 + width].astype(jnp.float32)
        lower = (block_id + 1) * (KW // 2)
        result = jnp.where(in_range[lower : lower + width][None, :], result, 0.0)
        activity = result.astype(jnp.bfloat16)
    part_height = C // mp_devices
    pieces = jnp.einsum(
        "jcd,jcf->jdf",
        dec_out_full.reshape(mp_devices, part_height, -1),
        activity.reshape(mp_devices, part_height, span),
        preferred_element_type=jnp.float32,
    )
    predicted = jnp.sum(rounded(pieces), axis=0)
    own_targets = lax.all_to_all(
        targets.reshape(targets.shape[0], mp_devices, span), "mp", 1, 0, tiled=True
    ).reshape(-1, span)
    own_keep = lax.dynamic_slice_in_dim(keep_flags, mp_index * span, span, 0)
    masked = (1 - own_keep).astype(jnp.float32)[None, :]
    own_error = ((predicted - own_targets.astype(jnp.float32)) * masked).astype(jnp.bfloat16)
    pred_error = lax.all_to_all(
        own_error.reshape(mp_devices, -1, span), "mp", 0, 2, tiled=True
    ).reshape(-1, frame_count)
    return (student_rows, pred_error)


def solution(mesh):
    return jax.shard_map(
        local,
        mesh=mesh,
        in_specs=(
            P("seq", "mp"),
            P("seq"),
            P("seq"),
            P(),
            P(None, None, "mp"),
            P("mp", None),
            P(None, "mp"),
            P("mp", None),
            P(),
            P(None, "mp"),
            P(None, None, "mp", None),
            P("mp", None),
            P("mp", "seq"),
        ),
        out_specs=(P("seq", "mp"), P("mp", "seq")),
        check_vma=False,
    )
```

```python
import math

import jax
import jax.numpy as jnp
from jax import lax
from jax.sharding import PartitionSpec as P

HEAD_DIM = 64
C = 768
CG = 48
KW = 7
BLOCKS = 4


NORM_EPSILON = 1e-05


def with_halo(block, sides, width):
    for axis, dim in sides:
        count = lax.axis_size(axis)
        forward = [(i, i + 1) for i in range(count - 1)]
        backward = [(target, source) for source, target in forward]
        low = lax.ppermute(
            lax.slice_in_dim(block, block.shape[dim] - width, None, axis=dim), axis, forward
        )
        high = lax.ppermute(lax.slice_in_dim(block, 0, width, axis=dim), axis, backward)
        block = jnp.concatenate([low, block, high], axis=dim)
    return block


def gather_all(values, axis):
    count = lax.axis_size(axis)
    spread = jnp.broadcast_to(values[None], (count,) + values.shape)
    return lax.all_to_all(spread, axis, 0, 0, tiled=True)


def sum_scatter(pieces, axis, dim):
    count = lax.axis_size(axis)
    shape = pieces.shape
    split = pieces.reshape(shape[:dim] + (count, shape[dim] // count) + shape[dim + 1 :])
    moved = lax.all_to_all(split, axis, dim, dim, tiled=True)
    return jnp.sum(moved.astype(jnp.float32), axis=dim)


def layer_norm(values, gain):
    values = values.astype(jnp.float32)
    centre = jnp.mean(values, axis=-1, keepdims=True)
    spread = jnp.mean(jnp.square(values - centre), axis=-1, keepdims=True)
    return (values - centre) * lax.rsqrt(spread + NORM_EPSILON) * gain


def rounded(values):
    return lax.optimization_barrier(values.astype(jnp.bfloat16)).astype(jnp.float32)


def local(
    frames,
    keep_flags,
    pack_rows,
    ln_gains,
    w_qkv,
    w_attn_out,
    w_up,
    w_down,
    mask_emb,
    w_dec_in,
    w_conv,
    w_dec_out,
    targets,
):
    frame_count = keep_flags.shape[0]
    slot_rows = pack_rows.shape[0]
    feature_width = frames.shape[1]
    seq_devices = lax.axis_size("seq")
    seq_index = lax.axis_index("seq")
    capacity = (2 * slot_rows + seq_devices - 1) // seq_devices
    kept_count = jnp.sum(keep_flags)
    counts_all = gather_all(kept_count[None], "seq").reshape(seq_devices)
    starts_all = jnp.cumsum(counts_all) - counts_all
    kept_before = starts_all[seq_index]
    local_rank = jnp.cumsum(keep_flags) - keep_flags
    frame_index = jnp.arange(frame_count, dtype=jnp.int32)
    kept_where = (
        jnp.zeros((frame_count,), jnp.int32)
        .at[jnp.where(keep_flags == 1, local_rank, frame_count)]
        .set(frame_index, mode="drop")
    )
    slot_steps = jnp.arange(capacity, dtype=jnp.int32)[None, :] * seq_devices
    owners = jnp.arange(seq_devices, dtype=jnp.int32)
    first_sent = kept_before + (owners - kept_before) % seq_devices
    offset = first_sent[:, None] + slot_steps - kept_before
    inside = offset < kept_count
    source = kept_where[jnp.clip(offset, 0, frame_count - 1)]
    outgoing = jnp.where(inside[..., None], frames[source], jnp.zeros((), jnp.bfloat16))
    incoming = lax.all_to_all(outgoing, "seq", split_axis=0, concat_axis=0, tiled=True)
    first_got = starts_all + (seq_index - starts_all) % seq_devices
    ranks_got = first_got[:, None] + slot_steps
    valid = ranks_got < (starts_all + counts_all)[:, None]
    places = jnp.where(valid, ranks_got // seq_devices, slot_rows).reshape(-1)
    by_rank = (
        jnp.zeros((slot_rows, feature_width), jnp.bfloat16)
        .at[places]
        .set(incoming.reshape(-1, feature_width), mode="drop")
    )
    local_row = pack_rows - seq_index * slot_rows
    inverse = (
        jnp.zeros((slot_rows,), jnp.int32).at[local_row].set(jnp.arange(slot_rows, dtype=jnp.int32))
    )
    packed = by_rank[inverse]
    heads_local = feature_width // HEAD_DIM
    gathered = lax.all_gather(packed, "mp", axis=1, tiled=True)
    normed = layer_norm(gathered, ln_gains[0]).astype(jnp.bfloat16)
    projected = jnp.dot(
        normed, w_qkv.reshape(w_qkv.shape[0], -1), preferred_element_type=jnp.float32
    ).astype(jnp.bfloat16)
    queries = projected[:, :feature_width].reshape(slot_rows, heads_local, HEAD_DIM)
    score_scale = 1.0 / math.sqrt(HEAD_DIM)
    start_state = (
        jnp.full((heads_local, slot_rows), -jnp.inf, jnp.float32),
        jnp.zeros((heads_local, slot_rows), jnp.float32),
        jnp.zeros((slot_rows, heads_local, HEAD_DIM), jnp.float32),
    )
    carry = start_state
    key_value = lax.all_gather(projected[:, feature_width:], "seq", axis=0, tiled=True)
    piece_keys = key_value[:, :feature_width]
    piece_values = key_value[:, feature_width:]
    piece_rows = piece_keys.shape[0]
    block_rows = math.gcd(piece_rows, 512)
    piece_keys = piece_keys.reshape(piece_rows // block_rows, block_rows, heads_local, HEAD_DIM)
    piece_values = piece_values.reshape(piece_rows // block_rows, block_rows, heads_local, HEAD_DIM)

    def advance(state, block_pair):
        running_max, totals, weighted = state
        block_keys, block_values = block_pair
        scores = (
            jnp.einsum("qhd,khd->hqk", queries, block_keys, preferred_element_type=jnp.float32)
            * score_scale
        )
        new_max = jnp.maximum(running_max, jnp.max(scores, axis=2))
        factor = jnp.exp(running_max - new_max)
        expo = jnp.exp(scores - new_max[:, :, None])
        totals = totals * factor + jnp.sum(expo, axis=2)
        weighted = weighted * jnp.transpose(factor)[:, :, None] + jnp.einsum(
            "hqk,khd->qhd",
            expo.astype(jnp.bfloat16),
            block_values,
            preferred_element_type=jnp.float32,
        )
        return ((new_max, totals, weighted), None)

    carry, _ = lax.scan(advance, carry, (piece_keys, piece_values))
    running_max, totals, weighted = carry
    attended = (
        (weighted / jnp.transpose(totals)[:, :, None])
        .reshape(slot_rows, feature_width)
        .astype(jnp.bfloat16)
    )
    attn_terms = rounded(jnp.dot(attended, w_attn_out, preferred_element_type=jnp.float32))
    attn_mixed = sum_scatter(attn_terms.astype(jnp.bfloat16), "mp", 1)
    first_out = (packed.astype(jnp.float32) + attn_mixed).astype(jnp.bfloat16)
    gathered_two = lax.all_gather(first_out, "mp", axis=1, tiled=True)
    normed_two = layer_norm(gathered_two, ln_gains[1]).astype(jnp.bfloat16)
    hidden = jax.nn.gelu(
        jnp.dot(normed_two, w_up, preferred_element_type=jnp.float32), approximate=False
    ).astype(jnp.bfloat16)
    mlp_terms = rounded(jnp.dot(hidden, w_down, preferred_element_type=jnp.float32))
    mlp_mixed = sum_scatter(mlp_terms.astype(jnp.bfloat16), "mp", 1)
    student_rows = (first_out.astype(jnp.float32) + mlp_mixed).astype(jnp.bfloat16)
    filler = lax.dynamic_slice_in_dim(
        mask_emb, lax.axis_index("mp") * feature_width, feature_width, 0
    )
    by_rank_out = student_rows[local_row]
    back_out = by_rank_out[jnp.clip(places, 0, slot_rows - 1)].reshape(
        seq_devices, capacity, feature_width
    )
    back_in = lax.all_to_all(back_out, "seq", 0, 0, tiled=True).reshape(-1, feature_width)
    back_index = ((kept_before + local_rank) % seq_devices) * capacity + local_rank // seq_devices
    returned = back_in[jnp.clip(back_index, 0, seq_devices * capacity - 1)]
    grid_rows = jnp.where(keep_flags[:, None] == 1, returned, filler[None, :])
    mp_devices = lax.axis_size("mp")
    mp_index = lax.axis_index("mp")
    span = frame_count // mp_devices
    halo = (KW // 2) * BLOCKS
    own_frames = lax.all_to_all(
        grid_rows.reshape(mp_devices, span, feature_width), "mp", 0, 2, tiled=True
    ).reshape(span, mp_devices * feature_width)
    dec_in_full = lax.all_gather(w_dec_in, "mp", axis=1, tiled=True)
    conv_full = lax.all_gather(
        w_conv.reshape(w_conv.shape[:2] + (-1, CG, CG)), "mp", axis=2, tiled=True
    )
    dec_out_full = lax.all_gather(w_dec_out, "mp", axis=0, tiled=True)
    activity = lax.dot_general(
        dec_in_full, own_frames, (((0,), (1,)), ((), ())), preferred_element_type=jnp.float32
    ).astype(jnp.bfloat16)
    both = ("seq", "mp")
    place = seq_index * mp_devices + mp_index
    places_total = seq_devices * mp_devices
    forward = [(i, i + 1) for i in range(places_total - 1)]
    backward = [(i + 1, i) for i in range(places_total - 1)]
    low = lax.ppermute(activity[:, span - halo :], both, forward)
    high = lax.ppermute(activity[:, :halo], both, backward)
    activity = jnp.concatenate([low, activity, high], axis=1)
    frame_at = place * span - halo + jnp.arange(span + 2 * halo, dtype=jnp.int32)
    in_range = (frame_at >= 0) & (frame_at < places_total * span)
    groups = C // CG
    for block_id in range(BLOCKS):
        width = activity.shape[1] - (KW - 1)
        kernel = conv_full[block_id]
        conv = jnp.zeros((groups, CG, width), jnp.float32)
        for tap_index in range(KW):
            tap = activity[:, tap_index : tap_index + width].reshape(groups, CG, width)
            conv = conv + jnp.einsum(
                "goi,gif->gof", kernel[tap_index], tap, preferred_element_type=jnp.float32
            )
        conv = conv.reshape(C, width)
        centre = jnp.mean(conv, axis=0)
        square_mean = jnp.mean(conv * conv, axis=0)
        normal = (conv - centre) * lax.rsqrt(square_mean - centre * centre + NORM_EPSILON)
        result = jax.nn.gelu(normal, approximate=False)
        if block_id > 0:
            result = result + activity[:, KW // 2 : KW // 2 + width].astype(jnp.float32)
        lower = (block_id + 1) * (KW // 2)
        result = jnp.where(in_range[lower : lower + width][None, :], result, 0.0)
        activity = result.astype(jnp.bfloat16)
    part_height = C // mp_devices
    pieces = jnp.einsum(
        "jcd,jcf->jdf",
        dec_out_full.reshape(mp_devices, part_height, -1),
        activity.reshape(mp_devices, part_height, span),
        preferred_element_type=jnp.float32,
    )
    predicted = jnp.sum(rounded(pieces), axis=0)
    own_targets = lax.all_to_all(
        targets.reshape(targets.shape[0], mp_devices, span), "mp", 1, 0, tiled=True
    ).reshape(-1, span)
    own_keep = lax.dynamic_slice_in_dim(keep_flags, mp_index * span, span, 0)
    masked = (1 - own_keep).astype(jnp.float32)[None, :]
    own_error = ((predicted - own_targets.astype(jnp.float32)) * masked).astype(jnp.bfloat16)
    pred_error = lax.all_to_all(
        own_error.reshape(mp_devices, -1, span), "mp", 0, 2, tiled=True
    ).reshape(-1, frame_count)
    return (student_rows, pred_error)


def solution(mesh):
    return jax.shard_map(
        local,
        mesh=mesh,
        in_specs=(
            P("seq", "mp"),
            P("seq"),
            P("seq"),
            P(),
            P(None, None, "mp"),
            P("mp", None),
            P(None, "mp"),
            P("mp", None),
            P(),
            P(None, "mp"),
            P(None, None, "mp", None),
            P("mp", None),
            P("mp", "seq"),
        ),
        out_specs=(P("seq", "mp"), P("mp", "seq")),
        check_vma=False,
    )
```

```python
import math

import jax
import jax.numpy as jnp
from jax import lax
from jax.sharding import PartitionSpec as P

HEAD_DIM = 64
C = 768
CG = 48
KW = 7
BLOCKS = 4


NORM_EPSILON = 1e-05


def with_halo(block, sides, width):
    for axis, dim in sides:
        count = lax.axis_size(axis)
        forward = [(i, i + 1) for i in range(count - 1)]
        backward = [(target, source) for source, target in forward]
        low = lax.ppermute(
            lax.slice_in_dim(block, block.shape[dim] - width, None, axis=dim), axis, forward
        )
        high = lax.ppermute(lax.slice_in_dim(block, 0, width, axis=dim), axis, backward)
        block = jnp.concatenate([low, block, high], axis=dim)
    return block


def gather_all(values, axis):
    count = lax.axis_size(axis)
    spread = jnp.broadcast_to(values[None], (count,) + values.shape)
    return lax.all_to_all(spread, axis, 0, 0, tiled=True)


def sum_scatter(pieces, axis, dim):
    count = lax.axis_size(axis)
    shape = pieces.shape
    split = pieces.reshape(shape[:dim] + (count, shape[dim] // count) + shape[dim + 1 :])
    moved = lax.all_to_all(split, axis, dim, dim, tiled=True)
    return jnp.sum(moved.astype(jnp.float32), axis=dim)


def layer_norm(values, gain):
    values = values.astype(jnp.float32)
    centre = jnp.mean(values, axis=-1, keepdims=True)
    spread = jnp.mean(jnp.square(values - centre), axis=-1, keepdims=True)
    return (values - centre) * lax.rsqrt(spread + NORM_EPSILON) * gain


def rounded(values):
    return lax.optimization_barrier(values.astype(jnp.bfloat16)).astype(jnp.float32)


def local(
    frames,
    keep_flags,
    pack_rows,
    ln_gains,
    w_qkv,
    w_attn_out,
    w_up,
    w_down,
    mask_emb,
    w_dec_in,
    w_conv,
    w_dec_out,
    targets,
):
    frame_count = keep_flags.shape[0]
    slot_rows = pack_rows.shape[0]
    feature_width = frames.shape[1]
    seq_devices = lax.axis_size("seq")
    seq_index = lax.axis_index("seq")
    capacity = (2 * slot_rows + seq_devices - 1) // seq_devices
    kept_count = jnp.sum(keep_flags)
    counts_all = gather_all(kept_count[None], "seq").reshape(seq_devices)
    starts_all = jnp.cumsum(counts_all) - counts_all
    kept_before = starts_all[seq_index]
    local_rank = jnp.cumsum(keep_flags) - keep_flags
    frame_index = jnp.arange(frame_count, dtype=jnp.int32)
    kept_where = (
        jnp.zeros((frame_count,), jnp.int32)
        .at[jnp.where(keep_flags == 1, local_rank, frame_count)]
        .set(frame_index, mode="drop")
    )
    slot_steps = jnp.arange(capacity, dtype=jnp.int32)[None, :] * seq_devices
    owners = jnp.arange(seq_devices, dtype=jnp.int32)
    first_sent = kept_before + (owners - kept_before) % seq_devices
    offset = first_sent[:, None] + slot_steps - kept_before
    inside = offset < kept_count
    source = kept_where[jnp.clip(offset, 0, frame_count - 1)]
    outgoing = jnp.where(inside[..., None], frames[source], jnp.zeros((), jnp.bfloat16))
    incoming = lax.all_to_all(outgoing, "seq", split_axis=0, concat_axis=0, tiled=True)
    first_got = starts_all + (seq_index - starts_all) % seq_devices
    ranks_got = first_got[:, None] + slot_steps
    valid = ranks_got < (starts_all + counts_all)[:, None]
    places = jnp.where(valid, ranks_got // seq_devices, slot_rows).reshape(-1)
    by_rank = (
        jnp.zeros((slot_rows, feature_width), jnp.bfloat16)
        .at[places]
        .set(incoming.reshape(-1, feature_width), mode="drop")
    )
    local_row = pack_rows - seq_index * slot_rows
    inverse = (
        jnp.zeros((slot_rows,), jnp.int32).at[local_row].set(jnp.arange(slot_rows, dtype=jnp.int32))
    )
    packed = by_rank[inverse]
    heads_local = feature_width // HEAD_DIM
    gathered = lax.all_gather(packed, "mp", axis=1, tiled=True)
    normed = layer_norm(gathered, ln_gains[0]).astype(jnp.bfloat16)
    projected = jnp.dot(
        normed, w_qkv.reshape(w_qkv.shape[0], -1), preferred_element_type=jnp.float32
    ).astype(jnp.bfloat16)
    queries = projected[:, :feature_width].reshape(slot_rows, heads_local, HEAD_DIM)
    score_scale = 1.0 / math.sqrt(HEAD_DIM)
    start_state = (
        jnp.full((heads_local, slot_rows), -jnp.inf, jnp.float32),
        jnp.zeros((heads_local, slot_rows), jnp.float32),
        jnp.zeros((slot_rows, heads_local, HEAD_DIM), jnp.float32),
    )
    carry = start_state
    key_value = lax.all_gather(projected[:, feature_width:], "seq", axis=0, tiled=True)
    piece_rows = key_value.shape[0]
    block_rows = math.gcd(piece_rows, 512)
    piece_pairs = key_value.reshape(piece_rows // block_rows, block_rows, 2, heads_local, HEAD_DIM)

    def advance(state, block_pair):
        running_max, totals, weighted = state
        block_keys = block_pair[:, 0]
        block_values = block_pair[:, 1]
        scores = (
            jnp.einsum("qhd,khd->hqk", queries, block_keys, preferred_element_type=jnp.float32)
            * score_scale
        )
        new_max = jnp.maximum(running_max, jnp.max(scores, axis=2))
        factor = jnp.exp(running_max - new_max)
        expo = jnp.exp(scores - new_max[:, :, None])
        totals = totals * factor + jnp.sum(expo, axis=2)
        weighted = weighted * jnp.transpose(factor)[:, :, None] + jnp.einsum(
            "hqk,khd->qhd",
            expo.astype(jnp.bfloat16),
            block_values,
            preferred_element_type=jnp.float32,
        )
        return ((new_max, totals, weighted), None)

    carry, _ = lax.scan(advance, carry, piece_pairs)
    running_max, totals, weighted = carry
    attended = (
        (weighted / jnp.transpose(totals)[:, :, None])
        .reshape(slot_rows, feature_width)
        .astype(jnp.bfloat16)
    )
    attn_terms = rounded(jnp.dot(attended, w_attn_out, preferred_element_type=jnp.float32))
    attn_mixed = sum_scatter(attn_terms.astype(jnp.bfloat16), "mp", 1)
    first_out = (packed.astype(jnp.float32) + attn_mixed).astype(jnp.bfloat16)
    gathered_two = lax.all_gather(first_out, "mp", axis=1, tiled=True)
    normed_two = layer_norm(gathered_two, ln_gains[1]).astype(jnp.bfloat16)
    hidden = jax.nn.gelu(
        jnp.dot(normed_two, w_up, preferred_element_type=jnp.float32), approximate=False
    ).astype(jnp.bfloat16)
    mlp_terms = rounded(jnp.dot(hidden, w_down, preferred_element_type=jnp.float32))
    mlp_mixed = sum_scatter(mlp_terms.astype(jnp.bfloat16), "mp", 1)
    student_rows = (first_out.astype(jnp.float32) + mlp_mixed).astype(jnp.bfloat16)
    filler = lax.dynamic_slice_in_dim(
        mask_emb, lax.axis_index("mp") * feature_width, feature_width, 0
    )
    by_rank_out = student_rows[local_row]
    back_out = by_rank_out[jnp.clip(places, 0, slot_rows - 1)].reshape(
        seq_devices, capacity, feature_width
    )
    back_in = lax.all_to_all(back_out, "seq", 0, 0, tiled=True).reshape(-1, feature_width)
    back_index = ((kept_before + local_rank) % seq_devices) * capacity + local_rank // seq_devices
    returned = back_in[jnp.clip(back_index, 0, seq_devices * capacity - 1)]
    grid_rows = jnp.where(keep_flags[:, None] == 1, returned, filler[None, :])
    mp_devices = lax.axis_size("mp")
    mp_index = lax.axis_index("mp")
    span = frame_count // mp_devices
    halo = (KW // 2) * BLOCKS
    own_frames = lax.all_to_all(
        grid_rows.reshape(mp_devices, span, feature_width), "mp", 0, 2, tiled=True
    ).reshape(span, mp_devices * feature_width)
    dec_in_full = lax.all_gather(w_dec_in, "mp", axis=1, tiled=True)
    conv_full = lax.all_gather(
        w_conv.reshape(w_conv.shape[:2] + (-1, CG, CG)), "mp", axis=2, tiled=True
    )
    dec_out_full = lax.all_gather(w_dec_out, "mp", axis=0, tiled=True)
    activity = lax.dot_general(
        dec_in_full, own_frames, (((0,), (1,)), ((), ())), preferred_element_type=jnp.float32
    ).astype(jnp.bfloat16)
    both = ("seq", "mp")
    place = seq_index * mp_devices + mp_index
    places_total = seq_devices * mp_devices
    forward = [(i, i + 1) for i in range(places_total - 1)]
    backward = [(i + 1, i) for i in range(places_total - 1)]
    low = lax.ppermute(activity[:, span - halo :], both, forward)
    high = lax.ppermute(activity[:, :halo], both, backward)
    activity = jnp.concatenate([low, activity, high], axis=1)
    frame_at = place * span - halo + jnp.arange(span + 2 * halo, dtype=jnp.int32)
    in_range = (frame_at >= 0) & (frame_at < places_total * span)
    groups = C // CG
    for block_id in range(BLOCKS):
        width = activity.shape[1] - (KW - 1)
        kernel = conv_full[block_id]
        conv = jnp.zeros((groups, CG, width), jnp.float32)
        for tap_index in range(KW):
            tap = activity[:, tap_index : tap_index + width].reshape(groups, CG, width)
            conv = conv + jnp.einsum(
                "goi,gif->gof", kernel[tap_index], tap, preferred_element_type=jnp.float32
            )
        conv = conv.reshape(C, width)
        centre = jnp.mean(conv, axis=0)
        square_mean = jnp.mean(conv * conv, axis=0)
        normal = (conv - centre) * lax.rsqrt(square_mean - centre * centre + NORM_EPSILON)
        result = jax.nn.gelu(normal, approximate=False)
        if block_id > 0:
            result = result + activity[:, KW // 2 : KW // 2 + width].astype(jnp.float32)
        lower = (block_id + 1) * (KW // 2)
        result = jnp.where(in_range[lower : lower + width][None, :], result, 0.0)
        activity = result.astype(jnp.bfloat16)
    part_height = C // mp_devices
    pieces = jnp.einsum(
        "jcd,jcf->jdf",
        dec_out_full.reshape(mp_devices, part_height, -1),
        activity.reshape(mp_devices, part_height, span),
        preferred_element_type=jnp.float32,
    )
    predicted = jnp.sum(rounded(pieces), axis=0)
    own_targets = lax.all_to_all(
        targets.reshape(targets.shape[0], mp_devices, span), "mp", 1, 0, tiled=True
    ).reshape(-1, span)
    own_keep = lax.dynamic_slice_in_dim(keep_flags, mp_index * span, span, 0)
    masked = (1 - own_keep).astype(jnp.float32)[None, :]
    own_error = ((predicted - own_targets.astype(jnp.float32)) * masked).astype(jnp.bfloat16)
    pred_error = lax.all_to_all(
        own_error.reshape(mp_devices, -1, span), "mp", 0, 2, tiled=True
    ).reshape(-1, frame_count)
    return (student_rows, pred_error)


def solution(mesh):
    return jax.shard_map(
        local,
        mesh=mesh,
        in_specs=(
            P("seq", "mp"),
            P("seq"),
            P("seq"),
            P(),
            P(None, None, "mp"),
            P("mp", None),
            P(None, "mp"),
            P("mp", None),
            P(),
            P(None, "mp"),
            P(None, None, "mp", None),
            P("mp", None),
            P("mp", "seq"),
        ),
        out_specs=(P("seq", "mp"), P("mp", "seq")),
        check_vma=False,
    )
```
